256 devices in a mesh: wide: 16 (over z, core), narrow: 16 (over x, y).
Axes of the slice: x: 4, y: 4, z: 8, core: 2. Of those that a mesh axis runs over, the one named last changes fastest.
Arguments:
- source: float32 [256, 2048, 128], P('wide', 'narrow'), may hold values from -14 to 14, as said below
- reaction: float32 [256, 2048, 128], P('wide', 'narrow'), may hold values from 0.02 to 0.2
- conductance: float32 [256, 2048, 128], P('wide', 'narrow'), may hold values from 0.25 to 2
- coarse_inverse: float32 [16, 16, 8, 2048], P('wide', 'narrow'), may hold values from -1 to 16, as said below
Outputs:
- solution: float32 [256, 2048, 128], P('wide', 'narrow')
- residual: float32 [256, 2048, 128], P('wide', 'narrow')
- direction: float32 [256, 2048, 128], P('wide', 'narrow')
The draws below stay inside these ranges and needn't reach their ends.
Inputs may be any that keep to these rules, and one draw needn't show every extreme that they name: source: finite values of either sign. coarse_inverse: a symmetric positive definite matrix.
All inputs are finite; a program needn't handle non-finite values.
Results may differ from the reference program's by a relative error of at most 0.0003.
Values sent between devices are 32-bit elements; how exact they have to be, the bound alone decides.
No kernel may reach another device: no remote copies, remote signals or barrier semaphores. Data moves between devices by JAX's collectives and lax.ppermute only.
A program may use at most 64 MiB of HBM per device.

```python
import math
import jax
import jax.numpy as jnp
from jax import lax

CX = 16
CY = 128
CZ = 128
W = 8
PRIMAL = 8
ITERS = 2
NX = 256
NY = 2048
NZ = 128
SUBS_W = 16
SUBS_N = 16
COARSE = 2048
N_WIDE = 16
N_NARROW = 16


def draw_source(key, part):
    key_rough, key_phase = jax.random.split(key)
    place_x = jnp.arange(NX, dtype=jnp.float32)[:, None, None] / NX
    place_y = jnp.arange(NY, dtype=jnp.float32)[None, :, None] / NY
    place_z = jnp.arange(NZ, dtype=jnp.float32)[None, None, :] / NZ
    phases = jax.random.uniform(key_phase, (3,), jnp.float32, 0.0, 6.283)
    smooth = 0.6 * jnp.sin(18.85 * place_x + phases[0]) * jnp.cos(12.566 * place_y + phases[1]) * jnp.cos(3.1416 * place_z + phases[2])
    ramp = 1.0 + 2.0 * place_x
    rough = jnp.clip(jax.random.normal(key_rough, (NX, NY, NZ), jnp.float32), -4.0, 4.0)
    return (ramp * (rough + smooth)).astype(jnp.float32)


def draw_coarse_inverse(key, part):
    key_diag, key_off = jax.random.split(key)
    diagonal = jnp.exp(jax.random.uniform(key_diag, (COARSE,), jnp.float32, 1.3863, 2.7725))
    uniform_raw = jax.random.uniform(key_off, (COARSE, COARSE), jnp.float32, -1.0, 1.0)
    symmetric = 0.5 * (uniform_raw + uniform_raw.T)
    scaling = jnp.sqrt(diagonal[:, None] * diagonal[None, :])
    off_scale = 0.5 / float(COARSE) ** 0.5
    identity_mask = jnp.arange(COARSE)[:, None] == jnp.arange(COARSE)[None, :]
    matrix = jnp.where(identity_mask, diagonal[:, None] * jnp.ones((1, COARSE), jnp.float32), off_scale * symmetric * scaling)
    return matrix.reshape(SUBS_W, SUBS_N, PRIMAL, COARSE).astype(jnp.float32)


def level_of(own_key, shape, pieces, smallest, high):
    factor_of = 1.0
    for dim, blocks in pieces:
        steps = jax.random.uniform(jax.random.fold_in(jax.random.fold_in(own_key, 6), dim), (blocks,), jnp.float32, smallest / len(pieces), high / len(pieces))
        factor_of = factor_of * jnp.repeat(jnp.exp(steps), shape[dim] // blocks).reshape((-1,) + (1,) * (len(shape) - 1 - dim))
    return factor_of


def setup_inputs(seed: int = 0) -> dict:
    seeds = jax.random.split(jax.random.key(seed), 5)
    source = draw_source(jax.random.fold_in(seeds[4], 71), 0)
    reaction = jnp.clip(jnp.exp(math.log(0.2) - 2.3025851 * jax.random.uniform(seeds[1], (NX, NY, NZ), jnp.float32) ** level_of(seeds[1], (NX, NY, NZ), ((0, 16), (1, 16)), -0.2, 0.2)), 0.02, 0.2)
    conductance = jnp.clip(jnp.exp(math.log(2.0) - 2.0794415 * jax.random.uniform(seeds[2], (NX, NY, NZ), jnp.float32) ** level_of(seeds[2], (NX, NY, NZ), ((0, 16), (1, 16)), -0.2, 0.2)), 0.25, 2.0)
    coarse_inverse = draw_coarse_inverse(jax.random.fold_in(seeds[4], 71), 0)
    return dict(source=source, reaction=reaction, conductance=conductance, coarse_inverse=coarse_inverse)


SHIFT = 0.06
KAPPA = 1.0

def sine_basis(extent):
    indices = jnp.arange(extent, dtype=jnp.float32) + 1.0
    angles = jnp.pi * indices[:, None] * indices[None, :] / (extent + 1)
    sine_table = jnp.sqrt(2.0 / (extent + 1)) * jnp.sin(angles)
    eigenvalues = 2.0 - 2.0 * jnp.cos(jnp.pi * indices / (extent + 1))
    return (sine_table, eigenvalues)

def harmonic(first, second):
    return 2.0 * first * second / (first + second)

def face_weights(padded_cond, conductance):
    face_x = harmonic(padded_cond[:-1, 1:-1], padded_cond[1:, 1:-1])
    face_y = harmonic(padded_cond[1:-1, :-1], padded_cond[1:-1, 1:])
    face_z = harmonic(conductance[:, :, :-1], conductance[:, :, 1:])
    return (face_x, face_y, face_z)

def operate(field, padded_field, reaction, face_x, face_y, face_z):
    result = reaction * field
    result = result + face_x[1:] * (field - padded_field[2:, 1:-1]) + face_x[:-1] * (field - padded_field[:-2, 1:-1])
    result = result + face_y[:, 1:] * (field - padded_field[1:-1, 2:]) + face_y[:, :-1] * (field - padded_field[1:-1, :-2])
    flux_z = face_z * (field[:, :, :-1] - field[:, :, 1:])
    return result + jnp.pad(flux_z, ((0, 0), (0, 0), (0, 1))) - jnp.pad(flux_z, ((0, 0), (0, 0), (1, 0)))

def transform_all(block, table_x, table_y, table_z):
    coeffs = jnp.einsum('rnyz,re->enyz', block, table_x, precision=lax.Precision.HIGHEST)
    coeffs = jnp.einsum('enyz,yb->enbz', coeffs, table_y, precision=lax.Precision.HIGHEST)
    return jnp.einsum('enbz,zc->enbc', coeffs, table_z, precision=lax.Precision.HIGHEST)

def local_solves(residual):
    extended = CX + 2 * W
    table_x, eigen_x = sine_basis(extended)
    table_y, eigen_y = sine_basis(CY)
    table_z, eigen_z = sine_basis(CZ)
    spectrum = SHIFT + KAPPA * (eigen_x[:, None, None, None] + eigen_y[None, None, :, None] + eigen_z[None, None, None, :])
    padded = jnp.pad(residual, ((W, W), (0, 0), (0, 0)))

    def one_slab(accumulated, position):
        offset_row = (position * CX).astype(jnp.int32)
        slab_block = lax.dynamic_slice_in_dim(padded, offset_row, extended, 0).reshape(extended, N_NARROW, CY, CZ)
        coeffs = transform_all(slab_block, table_x, table_y, table_z) / spectrum
        solved = transform_all(coeffs, table_x, table_y, table_z).reshape(extended, NY, NZ)
        current = lax.dynamic_slice_in_dim(accumulated, offset_row, extended, 0)
        return (lax.dynamic_update_slice_in_dim(accumulated, current + solved, offset_row, 0), None)
    accumulated, unused = lax.scan(one_slab, jnp.zeros_like(padded), jnp.arange(N_WIDE, dtype=jnp.int32))
    return accumulated[W:W + NX]

def coarse_part(residual, coarse_inverse):
    octant_means = residual.reshape(N_WIDE, 2, CX // 2, N_NARROW, 2, CY // 2, 2, CZ // 2).mean(axis=(2, 5, 7))
    ordered = octant_means.transpose(0, 2, 1, 3, 4).reshape(COARSE)
    correction = jnp.dot(coarse_inverse.reshape(COARSE, COARSE), ordered, precision=lax.Precision.HIGHEST)
    correction = correction.reshape(N_WIDE, N_NARROW, 2, 2, 2).transpose(0, 2, 1, 3, 4)
    spread = jnp.broadcast_to(correction[:, :, None, :, :, None, :, None], (N_WIDE, 2, CX // 2, N_NARROW, 2, CY // 2, 2, CZ // 2))
    return spread.reshape(NX, NY, NZ)

def reference(source, reaction, conductance, coarse_inverse):
    padded_cond = jnp.pad(conductance, ((1, 1), (1, 1), (0, 0)))
    face_x, face_y, face_z = face_weights(padded_cond, conductance)

    def apply_matrix(field):
        return operate(field, jnp.pad(field, ((1, 1), (1, 1), (0, 0))), reaction, face_x, face_y, face_z)

    def precondition(field):
        return local_solves(field) + coarse_part(field, coarse_inverse)
    solution = jnp.zeros_like(source)
    residual = source
    preconditioned = precondition(residual)
    direction = preconditioned
    gamma_now = jnp.sum(residual * preconditioned)
    for iteration in range(ITERS):
        image = apply_matrix(direction)
        step_size = gamma_now / jnp.sum(direction * image)
        solution = solution + step_size * direction
        residual = residual - step_size * image
        preconditioned = precondition(residual)
        gamma_next = jnp.sum(residual * preconditioned)
        direction = preconditioned + gamma_next / gamma_now * direction
        gamma_now = gamma_next
    return (solution, residual, direction)
```

```python
import jax
import jax.numpy as jnp
from jax import lax
from jax.sharding import PartitionSpec as P

W = 8
PRIMAL = 8
ITERS = 2


SHIFT = 0.06
KAPPA = 1.0


def with_halo(block, sides, width):
    for axis, dim in sides:
        count = lax.axis_size(axis)
        forward = [(i, i + 1) for i in range(count - 1)]
        backward = [(target, source) for source, target in forward]
        low = lax.ppermute(
            lax.slice_in_dim(block, block.shape[dim] - width, None, axis=dim), axis, forward
        )
        high = lax.ppermute(lax.slice_in_dim(block, 0, width, axis=dim), axis, backward)
        block = jnp.concatenate([low, block, high], axis=dim)
    return block


def passed_along(block, axis, distance):
    devices = range(lax.axis_size(axis))
    route = [(i - distance, i) for i in devices if i - distance in devices]
    return lax.ppermute(block, axis, route)


def tree_sum(values):
    while len(values) > 1:
        values = [values[i] + values[i + 1] for i in range(0, len(values), 2)]
    return values[0]


def total_over(value, axes=("wide", "narrow"), radix=4):
    for axis in axes:
        count = lax.axis_size(axis)
        stride = 1
        while stride < count:
            width = min(radix, count // stride)
            pulled = [
                lax.ppermute(value, axis, [(i, i ^ (j * stride)) for i in range(count)])
                for j in range(1, width)
            ]
            value = tree_sum([value] + pulled)
            stride *= width
    return value


def sine_basis(extent):
    indices = jnp.arange(extent, dtype=jnp.float32) + 1.0
    angles = jnp.pi * indices[:, None] * indices[None, :] / (extent + 1)
    sine_table = jnp.sqrt(2.0 / (extent + 1)) * jnp.sin(angles)
    eigenvalues = 2.0 - 2.0 * jnp.cos(jnp.pi * indices / (extent + 1))
    return (sine_table, eigenvalues)


def harmonic(first, second):
    return 2.0 * first * second / (first + second)


def face_weights(padded_cond, conductance):
    face_x = harmonic(padded_cond[:-1, 1:-1], padded_cond[1:, 1:-1])
    face_y = harmonic(padded_cond[1:-1, :-1], padded_cond[1:-1, 1:])
    face_z = harmonic(conductance[:, :, :-1], conductance[:, :, 1:])
    return (face_x, face_y, face_z)


def operate(field, padded_field, reaction, face_x, face_y, face_z):
    result = reaction * field
    result = (
        result
        + face_x[1:] * (field - padded_field[2:, 1:-1])
        + face_x[:-1] * (field - padded_field[:-2, 1:-1])
    )
    result = (
        result
        + face_y[:, 1:] * (field - padded_field[1:-1, 2:])
        + face_y[:, :-1] * (field - padded_field[1:-1, :-2])
    )
    flux_z = face_z * (field[:, :, :-1] - field[:, :, 1:])
    return (
        result
        + jnp.pad(flux_z, ((0, 0), (0, 0), (0, 1)))
        - jnp.pad(flux_z, ((0, 0), (0, 0), (1, 0)))
    )


def transform_first(field, table_x):
    return jnp.einsum("ryz,re->eyz", field, table_x, precision=lax.Precision.HIGHEST)


def transform_cross(field, table_y, table_z):
    inner = jnp.einsum("ryz,zc->ryc", field, table_z, precision=lax.Precision.HIGHEST)
    return jnp.einsum("ryc,yb->rbc", inner, table_y, precision=lax.Precision.HIGHEST)


def body(source, reaction, conductance, coarse_inverse):
    block_x, block_y, block_z = source.shape
    extended = block_x + 2 * W
    padded_cond = with_halo(conductance, (("wide", 0), ("narrow", 1)), 1)
    face_x, face_y, face_z = face_weights(padded_cond, conductance)
    table_x, eigen_x = sine_basis(extended)
    table_y, eigen_y = sine_basis(block_y)
    table_z, eigen_z = sine_basis(block_z)
    spectrum = SHIFT + KAPPA * (
        eigen_x[:, None, None] + eigen_y[None, :, None] + eigen_z[None, None, :]
    )
    coarse_rows = coarse_inverse.reshape(PRIMAL, -1)

    def widen(field):
        return with_halo(field, (("wide", 0),), W)

    def fold_back(solved):
        owned = solved[W : W + block_x]
        for offset in (1, -1):
            rim_piece = solved[W + block_x :] if offset == 1 else solved[:W]
            arrived = passed_along(rim_piece, "wide", offset)
            if offset == 1:
                owned = owned + jnp.pad(arrived, ((0, block_x - W), (0, 0), (0, 0)))
            else:
                owned = owned + jnp.pad(arrived, ((block_x - W, 0), (0, 0), (0, 0)))
        return owned

    def precondition(field):
        coeffs = (
            transform_cross(transform_first(widen(field), table_x), table_y, table_z) / spectrum
        )
        local_part = fold_back(transform_cross(transform_first(coeffs, table_x), table_y, table_z))
        octant_means = (
            field.reshape(2, block_x // 2, 2, block_y // 2, 2, block_z // 2)
            .mean(axis=(1, 3, 5))
            .reshape(PRIMAL)
        )
        slot = lax.axis_index("wide") * lax.axis_size("narrow") + lax.axis_index("narrow")
        placed = lax.dynamic_update_slice(
            jnp.zeros((coarse_rows.shape[1],), octant_means.dtype), octant_means, (slot * PRIMAL,)
        )
        all_means = total_over(placed)
        correction = jnp.dot(coarse_rows, all_means, precision=lax.Precision.HIGHEST).reshape(
            2, 2, 2
        )
        spread = jnp.broadcast_to(
            correction[:, None, :, None, :, None],
            (2, block_x // 2, 2, block_y // 2, 2, block_z // 2),
        )
        return local_part + spread.reshape(block_x, block_y, block_z)

    def inner_norm(residual, preconditioned):
        return total_over(jnp.sum(residual * preconditioned))

    solution = jnp.zeros_like(source)
    residual = source
    preconditioned = precondition(residual)
    direction = preconditioned
    gamma_now = None
    for iteration in range(ITERS):
        padded_field = with_halo(direction, (("wide", 0), ("narrow", 1)), 1)
        image = operate(direction, padded_field, reaction, face_x, face_y, face_z)
        if gamma_now is None:
            both = total_over(
                jnp.stack([jnp.sum(residual * preconditioned), jnp.sum(direction * image)])
            )
            gamma_now, curvature = both[0], both[1]
        else:
            curvature = total_over(jnp.sum(direction * image))
        step_size = gamma_now / curvature
        solution = solution + step_size * direction
        residual = residual - step_size * image
        preconditioned = precondition(residual)
        gamma_next = inner_norm(residual, preconditioned)
        direction = preconditioned + gamma_next / gamma_now * direction
        gamma_now = gamma_next
    return (solution, residual, direction)


def solution(mesh):
    in_specs = (
        P("wide", "narrow", None),
        P("wide", "narrow", None),
        P("wide", "narrow", None),
        P("wide", "narrow", None, None),
    )
    out_specs = (P("wide", "narrow", None), P("wide", "narrow", None), P("wide", "narrow", None))
    return jax.shard_map(body, mesh=mesh, in_specs=in_specs, out_specs=out_specs, check_vma=False)
```

```python
import jax
import jax.numpy as jnp
from jax import lax
from jax.sharding import PartitionSpec as P

W = 8
PRIMAL = 8
ITERS = 2


SHIFT = 0.06
KAPPA = 1.0


def with_halo(block, sides, width):
    for axis, dim in sides:
        count = lax.axis_size(axis)
        forward = [(i, i + 1) for i in range(count - 1)]
        backward = [(target, source) for source, target in forward]
        low = lax.ppermute(
            lax.slice_in_dim(block, block.shape[dim] - width, None, axis=dim), axis, forward
        )
        high = lax.ppermute(lax.slice_in_dim(block, 0, width, axis=dim), axis, backward)
        block = jnp.concatenate([low, block, high], axis=dim)
    return block


def passed_along(block, axis, distance):
    devices = range(lax.axis_size(axis))
    route = [(i - distance, i) for i in devices if i - distance in devices]
    return lax.ppermute(block, axis, route)


def tree_sum(values):
    while len(values) > 1:
        values = [values[i] + values[i + 1] for i in range(0, len(values), 2)]
    return values[0]


def total_over(value, axes=("wide", "narrow"), radix=4):
    for axis in axes:
        count = lax.axis_size(axis)
        stride = 1
        while stride < count:
            width = min(radix, count // stride)
            pulled = [
                lax.ppermute(value, axis, [(i, i ^ (j * stride)) for i in range(count)])
                for j in range(1, width)
            ]
            value = tree_sum([value] + pulled)
            stride *= width
    return value


def sine_basis(extent):
    indices = jnp.arange(extent, dtype=jnp.float32) + 1.0
    angles = jnp.pi * indices[:, None] * indices[None, :] / (extent + 1)
    sine_table = jnp.sqrt(2.0 / (extent + 1)) * jnp.sin(angles)
    eigenvalues = 2.0 - 2.0 * jnp.cos(jnp.pi * indices / (extent + 1))
    return (sine_table, eigenvalues)


def harmonic(first, second):
    return 2.0 * first * second / (first + second)


def face_weights(padded_cond, conductance):
    face_x = harmonic(padded_cond[:-1, 1:-1], padded_cond[1:, 1:-1])
    face_y = harmonic(padded_cond[1:-1, :-1], padded_cond[1:-1, 1:])
    face_z = harmonic(conductance[:, :, :-1], conductance[:, :, 1:])
    return (face_x, face_y, face_z)


def operate(field, padded_field, reaction, face_x, face_y, face_z):
    result = reaction * field
    result = (
        result
        + face_x[1:] * (field - padded_field[2:, 1:-1])
        + face_x[:-1] * (field - padded_field[:-2, 1:-1])
    )
    result = (
        result
        + face_y[:, 1:] * (field - padded_field[1:-1, 2:])
        + face_y[:, :-1] * (field - padded_field[1:-1, :-2])
    )
    flux_z = face_z * (field[:, :, :-1] - field[:, :, 1:])
    return (
        result
        + jnp.pad(flux_z, ((0, 0), (0, 0), (0, 1)))
        - jnp.pad(flux_z, ((0, 0), (0, 0), (1, 0)))
    )


def transform_first(field, table_x):
    return jnp.einsum("ryz,re->eyz", field, table_x, precision=lax.Precision.HIGHEST)


def transform_cross(field, table_y, table_z):
    inner = jnp.einsum("ryz,zc->ryc", field, table_z, precision=lax.Precision.HIGHEST)
    return jnp.einsum("ryc,yb->rbc", inner, table_y, precision=lax.Precision.HIGHEST)


def body(source, reaction, conductance, coarse_inverse):
    block_x, block_y, block_z = source.shape
    extended = block_x + 2 * W
    padded_cond = with_halo(conductance, (("wide", 0), ("narrow", 1)), 1)
    face_x, face_y, face_z = face_weights(padded_cond, conductance)
    table_x, eigen_x = sine_basis(extended)
    table_y, eigen_y = sine_basis(block_y)
    table_z, eigen_z = sine_basis(block_z)
    spectrum = SHIFT + KAPPA * (
        eigen_x[:, None, None] + eigen_y[None, :, None] + eigen_z[None, None, :]
    )
    coarse_rows = coarse_inverse.reshape(PRIMAL, -1)

    def widen(field):
        return with_halo(field, (("wide", 0),), W)

    def fold_back(solved):
        owned = solved[W : W + block_x]
        for offset in (1, -1):
            rim_piece = solved[W + block_x :] if offset == 1 else solved[:W]
            arrived = passed_along(rim_piece, "wide", offset)
            if offset == 1:
                owned = owned + jnp.pad(arrived, ((0, block_x - W), (0, 0), (0, 0)))
            else:
                owned = owned + jnp.pad(arrived, ((block_x - W, 0), (0, 0), (0, 0)))
        return owned

    slot = lax.axis_index("wide") * lax.axis_size("narrow") + lax.axis_index("narrow")

    def placed_means(field):
        octant_means = (
            field.reshape(2, block_x // 2, 2, block_y // 2, 2, block_z // 2)
            .mean(axis=(1, 3, 5))
            .reshape(PRIMAL)
        )
        return lax.dynamic_update_slice(
            jnp.zeros((coarse_rows.shape[1],), octant_means.dtype), octant_means, (slot * PRIMAL,)
        )

    def precondition(field, all_means):
        coeffs = (
            transform_cross(transform_first(widen(field), table_x), table_y, table_z) / spectrum
        )
        local_part = fold_back(transform_cross(transform_first(coeffs, table_x), table_y, table_z))
        correction = jnp.dot(coarse_rows, all_means, precision=lax.Precision.HIGHEST).reshape(
            2, 2, 2
        )
        spread = jnp.broadcast_to(
            correction[:, None, :, None, :, None],
            (2, block_x // 2, 2, block_y // 2, 2, block_z // 2),
        )
        return local_part + spread.reshape(block_x, block_y, block_z)

    def apply_matrix(field):
        padded_field = with_halo(field, (("wide", 0), ("narrow", 1)), 1)
        return operate(field, padded_field, reaction, face_x, face_y, face_z)

    residual = source
    residual_means = total_over(placed_means(residual))
    preconditioned = precondition(residual, residual_means)
    bent = apply_matrix(preconditioned)
    sums = total_over(
        jnp.concatenate(
            [
                jnp.stack([jnp.sum(residual * preconditioned), jnp.sum(preconditioned * bent)]),
                placed_means(bent),
            ]
        )
    )
    gamma_now, curvature, image_means = sums[0], sums[1], sums[2:]
    direction, image = preconditioned, bent
    step_size = gamma_now / curvature
    solution = step_size * direction
    residual = residual - step_size * image
    residual_means = residual_means - step_size * image_means
    for iteration in range(1, ITERS):
        preconditioned = precondition(residual, residual_means)
        bent = apply_matrix(preconditioned)
        sums = total_over(
            jnp.concatenate(
                [
                    jnp.stack(
                        [
                            jnp.sum(residual * preconditioned),
                            jnp.sum(preconditioned * bent),
                            jnp.sum(preconditioned * image),
                            jnp.sum(direction * bent),
                        ]
                    ),
                    placed_means(bent),
                ]
            )
        )
        gamma_next = sums[0]
        ratio = gamma_next / gamma_now
        curvature = sums[1] + ratio * (sums[2] + sums[3]) + ratio * ratio * curvature
        direction = preconditioned + ratio * direction
        image = bent + ratio * image
        image_means = sums[4:] + ratio * image_means
        gamma_now = gamma_next
        step_size = gamma_now / curvature
        solution = solution + step_size * direction
        residual = residual - step_size * image
        residual_means = residual_means - step_size * image_means
    preconditioned = precondition(residual, residual_means)
    gamma_next = total_over(jnp.sum(residual * preconditioned))
    direction = preconditioned + gamma_next / gamma_now * direction
    return (solution, residual, direction)


def solution(mesh):
    in_specs = (
        P("wide", "narrow", None),
        P("wide", "narrow", None),
        P("wide", "narrow", None),
        P("wide", "narrow", None, None),
    )
    out_specs = (P("wide", "narrow", None), P("wide", "narrow", None), P("wide", "narrow", None))
    return jax.shard_map(body, mesh=mesh, in_specs=in_specs, out_specs=out_specs, check_vma=False)
```

```python
import jax
import jax.numpy as jnp
from jax import lax
from jax.sharding import PartitionSpec as P

W = 8
PRIMAL = 8
ITERS = 2


SHIFT = 0.06
KAPPA = 1.0


def with_halo(block, sides, width):
    for axis, dim in sides:
        count = lax.axis_size(axis)
        forward = [(i, i + 1) for i in range(count - 1)]
        backward = [(target, source) for source, target in forward]
        low = lax.ppermute(
            lax.slice_in_dim(block, block.shape[dim] - width, None, axis=dim), axis, forward
        )
        high = lax.ppermute(lax.slice_in_dim(block, 0, width, axis=dim), axis, backward)
        block = jnp.concatenate([low, block, high], axis=dim)
    return block


def passed_along(block, axis, distance):
    devices = range(lax.axis_size(axis))
    route = [(i - distance, i) for i in devices if i - distance in devices]
    return lax.ppermute(block, axis, route)


def tree_sum(values):
    while len(values) > 1:
        values = [values[i] + values[i + 1] for i in range(0, len(values), 2)]
    return values[0]


def total_over(value, axes=("wide", "narrow"), radix=4):
    for axis in axes:
        count = lax.axis_size(axis)
        stride = 1
        while stride < count:
            width = min(radix, count // stride)
            pulled = [
                lax.ppermute(value, axis, [(i, i ^ (j * stride)) for i in range(count)])
                for j in range(1, width)
            ]
            value = tree_sum([value] + pulled)
            stride *= width
    return value


def sine_basis(extent):
    indices = jnp.arange(extent, dtype=jnp.float32) + 1.0
    angles = jnp.pi * indices[:, None] * indices[None, :] / (extent + 1)
    sine_table = jnp.sqrt(2.0 / (extent + 1)) * jnp.sin(angles)
    eigenvalues = 2.0 - 2.0 * jnp.cos(jnp.pi * indices / (extent + 1))
    return (sine_table, eigenvalues)


def harmonic(first, second):
    return 2.0 * first * second / (first + second)


def face_weights(padded_cond, conductance):
    face_x = harmonic(padded_cond[:-1, 1:-1], padded_cond[1:, 1:-1])
    face_y = harmonic(padded_cond[1:-1, :-1], padded_cond[1:-1, 1:])
    face_z = harmonic(conductance[:, :, :-1], conductance[:, :, 1:])
    return (face_x, face_y, face_z)


def operate(field, padded_field, reaction, face_x, face_y, face_z):
    result = reaction * field
    result = (
        result
        + face_x[1:] * (field - padded_field[2:, 1:-1])
        + face_x[:-1] * (field - padded_field[:-2, 1:-1])
    )
    result = (
        result
        + face_y[:, 1:] * (field - padded_field[1:-1, 2:])
        + face_y[:, :-1] * (field - padded_field[1:-1, :-2])
    )
    flux_z = face_z * (field[:, :, :-1] - field[:, :, 1:])
    return (
        result
        + jnp.pad(flux_z, ((0, 0), (0, 0), (0, 1)))
        - jnp.pad(flux_z, ((0, 0), (0, 0), (1, 0)))
    )


def transform_first(field, table_x):
    return jnp.einsum("ryz,re->eyz", field, table_x, precision=lax.Precision.HIGHEST)


def transform_cross(field, table_y, table_z):
    inner = jnp.einsum("ryz,zc->ryc", field, table_z, precision=lax.Precision.HIGHEST)
    return jnp.einsum("ryc,yb->rbc", inner, table_y, precision=lax.Precision.HIGHEST)


def body(source, reaction, conductance, coarse_inverse):
    block_x, block_y, block_z = source.shape
    extended = block_x + 2 * W
    padded_cond = with_halo(conductance, (("wide", 0), ("narrow", 1)), 1)
    face_x, face_y, face_z = face_weights(padded_cond, conductance)
    table_x, eigen_x = sine_basis(extended)
    table_y, eigen_y = sine_basis(block_y)
    table_z, eigen_z = sine_basis(block_z)
    spectrum = SHIFT + KAPPA * (
        eigen_x[:, None, None] + eigen_y[None, :, None] + eigen_z[None, None, :]
    )
    coarse_rows = coarse_inverse.reshape(PRIMAL, -1)

    def widen(field):
        return with_halo(field, (("wide", 0),), W)

    def fold_back(solved):
        owned = solved[W : W + block_x]
        for offset in (1, -1):
            rim_piece = solved[W + block_x :] if offset == 1 else solved[:W]
            arrived = passed_along(rim_piece, "wide", offset)
            if offset == 1:
                owned = owned + jnp.pad(arrived, ((0, block_x - W), (0, 0), (0, 0)))
            else:
                owned = owned + jnp.pad(arrived, ((block_x - W, 0), (0, 0), (0, 0)))
        return owned

    slot = lax.axis_index("wide") * lax.axis_size("narrow") + lax.axis_index("narrow")

    def placed_means(field):
        along_x = field.reshape(2, block_x // 2, block_y, block_z).sum(axis=1)
        along_y = along_x.reshape(2, 2, block_y // 2, block_z).sum(axis=2)
        along_z = along_y.reshape(2, 2, 2, block_z // 2).sum(axis=3)
        octant_means = (along_z / ((block_x // 2) * (block_y // 2) * (block_z // 2))).reshape(PRIMAL)
        return lax.dynamic_update_slice(
            jnp.zeros((coarse_rows.shape[1],), octant_means.dtype), octant_means, (slot * PRIMAL,)
        )

    def precondition(field, all_means):
        coeffs = (
            transform_cross(transform_first(widen(field), table_x), table_y, table_z) / spectrum
        )
        local_part = fold_back(transform_cross(transform_first(coeffs, table_x), table_y, table_z))
        correction = jnp.dot(coarse_rows, all_means, precision=lax.Precision.HIGHEST).reshape(
            2, 2, 2
        )
        upper_z = lax.broadcasted_iota(jnp.int32, (1, 1, block_z), 2) >= block_z // 2
        rows = jnp.where(upper_z, correction[:, :, 1:2], correction[:, :, 0:1])
        spread = jnp.broadcast_to(
            rows[:, None, :, None, :], (2, block_x // 2, 2, block_y // 2, block_z)
        )
        return local_part + spread.reshape(block_x, block_y, block_z)

    def apply_matrix(field):
        padded_field = with_halo(field, (("wide", 0), ("narrow", 1)), 1)
        return operate(field, padded_field, reaction, face_x, face_y, face_z)

    residual = source
    residual_means = total_over(placed_means(residual))
    preconditioned = precondition(residual, residual_means)
    bent = apply_matrix(preconditioned)
    sums = total_over(
        jnp.concatenate(
            [
                jnp.stack([jnp.sum(residual * preconditioned), jnp.sum(preconditioned * bent)]),
                placed_means(bent),
            ]
        )
    )
    gamma_now, curvature, image_means = sums[0], sums[1], sums[2:]
    direction, image = preconditioned, bent
    step_size = gamma_now / curvature
    solution = step_size * direction
    residual = residual - step_size * image
    residual_means = residual_means - step_size * image_means
    for iteration in range(1, ITERS):
        preconditioned = precondition(residual, residual_means)
        bent = apply_matrix(preconditioned)
        sums = total_over(
            jnp.concatenate(
                [
                    jnp.stack(
                        [
                            jnp.sum(residual * preconditioned),
                            jnp.sum(preconditioned * bent),
                            jnp.sum(preconditioned * image),
                            jnp.sum(direction * bent),
                        ]
                    ),
                    placed_means(bent),
                ]
            )
        )
        gamma_next = sums[0]
        ratio = gamma_next / gamma_now
        curvature = sums[1] + ratio * (sums[2] + sums[3]) + ratio * ratio * curvature
        direction = preconditioned + ratio * direction
        image = bent + ratio * image
        image_means = sums[4:] + ratio * image_means
        gamma_now = gamma_next
        step_size = gamma_now / curvature
        solution = solution + step_size * direction
        residual = residual - step_size * image
        residual_means = residual_means - step_size * image_means
    preconditioned = precondition(residual, residual_means)
    gamma_next = total_over(jnp.sum(residual * preconditioned))
    direction = preconditioned + gamma_next / gamma_now * direction
    return (solution, residual, direction)


def solution(mesh):
    in_specs = (
        P("wide", "narrow", None),
        P("wide", "narrow", None),
        P("wide", "narrow", None),
        P("wide", "narrow", None, None),
    )
    out_specs = (P("wide", "narrow", None), P("wide", "narrow", None), P("wide", "narrow", None))
    return jax.shard_map(body, mesh=mesh, in_specs=in_specs, out_specs=out_specs, check_vma=False)
```

```python
import jax
import jax.numpy as jnp
from jax import lax
from jax.sharding import PartitionSpec as P

W = 8
PRIMAL = 8
ITERS = 2


SHIFT = 0.06
TRANSFORM_PRECISION = lax.Precision.HIGH
KAPPA = 1.0


def with_halo(block, sides, width):
    for axis, dim in sides:
        count = lax.axis_size(axis)
        forward = [(i, i + 1) for i in range(count - 1)]
        backward = [(target, source) for source, target in forward]
        low = lax.ppermute(
            lax.slice_in_dim(block, block.shape[dim] - width, None, axis=dim), axis, forward
        )
        high = lax.ppermute(lax.slice_in_dim(block, 0, width, axis=dim), axis, backward)
        block = jnp.concatenate([low, block, high], axis=dim)
    return block


def passed_along(block, axis, distance):
    devices = range(lax.axis_size(axis))
    route = [(i - distance, i) for i in devices if i - distance in devices]
    return lax.ppermute(block, axis, route)


def tree_sum(values):
    while len(values) > 1:
        values = [values[i] + values[i + 1] for i in range(0, len(values), 2)]
    return values[0]


def total_over(value, axes=("wide", "narrow"), radix=4):
    for axis in axes:
        count = lax.axis_size(axis)
        stride = 1
        while stride < count:
            width = min(radix, count // stride)
            pulled = [
                lax.ppermute(value, axis, [(i, i ^ (j * stride)) for i in range(count)])
                for j in range(1, width)
            ]
            value = tree_sum([value] + pulled)
            stride *= width
    return value


def sine_basis(extent):
    indices = jnp.arange(extent, dtype=jnp.float32) + 1.0
    angles = jnp.pi * indices[:, None] * indices[None, :] / (extent + 1)
    sine_table = jnp.sqrt(2.0 / (extent + 1)) * jnp.sin(angles)
    eigenvalues = 2.0 - 2.0 * jnp.cos(jnp.pi * indices / (extent + 1))
    return (sine_table, eigenvalues)


def harmonic(first, second):
    return 2.0 * first * second / (first + second)


def face_weights(padded_cond, conductance):
    face_x = harmonic(padded_cond[:-1, 1:-1], padded_cond[1:, 1:-1])
    face_y = harmonic(padded_cond[1:-1, :-1], padded_cond[1:-1, 1:])
    face_z = harmonic(conductance[:, :, :-1], conductance[:, :, 1:])
    return (face_x, face_y, face_z)


def operate(field, padded_field, reaction, face_x, face_y, face_z):
    result = reaction * field
    result = (
        result
        + face_x[1:] * (field - padded_field[2:, 1:-1])
        + face_x[:-1] * (field - padded_field[:-2, 1:-1])
    )
    result = (
        result
        + face_y[:, 1:] * (field - padded_field[1:-1, 2:])
        + face_y[:, :-1] * (field - padded_field[1:-1, :-2])
    )
    flux_z = face_z * (field[:, :, :-1] - field[:, :, 1:])
    return (
        result
        + jnp.pad(flux_z, ((0, 0), (0, 0), (0, 1)))
        - jnp.pad(flux_z, ((0, 0), (0, 0), (1, 0)))
    )


def transform_first(field, table_x):
    return jnp.einsum("ryz,re->eyz", field, table_x, precision=TRANSFORM_PRECISION)


def transform_cross(field, table_y, table_z):
    inner = jnp.einsum("ryz,zc->ryc", field, table_z, precision=TRANSFORM_PRECISION)
    return jnp.einsum("ryc,yb->rbc", inner, table_y, precision=TRANSFORM_PRECISION)


def body(source, reaction, conductance, coarse_inverse):
    block_x, block_y, block_z = source.shape
    extended = block_x + 2 * W
    padded_cond = with_halo(conductance, (("wide", 0), ("narrow", 1)), 1)
    face_x, face_y, face_z = face_weights(padded_cond, conductance)
    table_x, eigen_x = sine_basis(extended)
    table_y, eigen_y = sine_basis(block_y)
    table_z, eigen_z = sine_basis(block_z)
    spectrum = SHIFT + KAPPA * (
        eigen_x[:, None, None] + eigen_y[None, :, None] + eigen_z[None, None, :]
    )
    coarse_rows = coarse_inverse.reshape(PRIMAL, -1)

    def widen(field):
        return with_halo(field, (("wide", 0),), W)

    def fold_back(solved):
        owned = solved[W : W + block_x]
        for offset in (1, -1):
            rim_piece = solved[W + block_x :] if offset == 1 else solved[:W]
            arrived = passed_along(rim_piece, "wide", offset)
            if offset == 1:
                owned = owned + jnp.pad(arrived, ((0, block_x - W), (0, 0), (0, 0)))
            else:
                owned = owned + jnp.pad(arrived, ((block_x - W, 0), (0, 0), (0, 0)))
        return owned

    slot = lax.axis_index("wide") * lax.axis_size("narrow") + lax.axis_index("narrow")

    def placed_means(field):
        along_x = field.reshape(2, block_x // 2, block_y, block_z).sum(axis=1)
        along_y = along_x.reshape(2, 2, block_y // 2, block_z).sum(axis=2)
        along_z = along_y.reshape(2, 2, 2, block_z // 2).sum(axis=3)
        octant_means = (along_z / ((block_x // 2) * (block_y // 2) * (block_z // 2))).reshape(PRIMAL)
        return lax.dynamic_update_slice(
            jnp.zeros((coarse_rows.shape[1],), octant_means.dtype), octant_means, (slot * PRIMAL,)
        )

    def precondition(field, all_means):
        coeffs = (
            transform_cross(transform_first(widen(field), table_x), table_y, table_z) / spectrum
        )
        local_part = fold_back(transform_cross(transform_first(coeffs, table_x), table_y, table_z))
        correction = jnp.dot(coarse_rows, all_means, precision=lax.Precision.HIGHEST).reshape(
            2, 2, 2
        )
        upper_z = lax.broadcasted_iota(jnp.int32, (1, 1, block_z), 2) >= block_z // 2
        rows = jnp.where(upper_z, correction[:, :, 1:2], correction[:, :, 0:1])
        spread = jnp.broadcast_to(
            rows[:, None, :, None, :], (2, block_x // 2, 2, block_y // 2, block_z)
        )
        return local_part + spread.reshape(block_x, block_y, block_z)

    def apply_matrix(field):
        padded_field = with_halo(field, (("wide", 0), ("narrow", 1)), 1)
        return operate(field, padded_field, reaction, face_x, face_y, face_z)

    residual = source
    residual_means = total_over(placed_means(residual))
    preconditioned = precondition(residual, residual_means)
    bent = apply_matrix(preconditioned)
    sums = total_over(
        jnp.concatenate(
            [
                jnp.stack([jnp.sum(residual * preconditioned), jnp.sum(preconditioned * bent)]),
                placed_means(bent),
            ]
        )
    )
    gamma_now, curvature, image_means = sums[0], sums[1], sums[2:]
    direction, image = preconditioned, bent
    step_size = gamma_now / curvature
    solution = step_size * direction
    residual = residual - step_size * image
    residual_means = residual_means - step_size * image_means
    for iteration in range(1, ITERS):
        preconditioned = precondition(residual, residual_means)
        bent = apply_matrix(preconditioned)
        sums = total_over(
            jnp.concatenate(
                [
                    jnp.stack(
                        [
                            jnp.sum(residual * preconditioned),
                            jnp.sum(preconditioned * bent),
                            jnp.sum(preconditioned * image),
                            jnp.sum(direction * bent),
                        ]
                    ),
                    placed_means(bent),
                ]
            )
        )
        gamma_next = sums[0]
        ratio = gamma_next / gamma_now
        curvature = sums[1] + ratio * (sums[2] + sums[3]) + ratio * ratio * curvature
        direction = preconditioned + ratio * direction
        image = bent + ratio * image
        image_means = sums[4:] + ratio * image_means
        gamma_now = gamma_next
        step_size = gamma_now / curvature
        solution = solution + step_size * direction
        residual = residual - step_size * image
        residual_means = residual_means - step_size * image_means
    preconditioned = precondition(residual, residual_means)
    gamma_next = total_over(jnp.sum(residual * preconditioned))
    direction = preconditioned + gamma_next / gamma_now * direction
    return (solution, residual, direction)


def solution(mesh):
    in_specs = (
        P("wide", "narrow", None),
        P("wide", "narrow", None),
        P("wide", "narrow", None),
        P("wide", "narrow", None, None),
    )
    out_specs = (P("wide", "narrow", None), P("wide", "narrow", None), P("wide", "narrow", None))
    return jax.shard_map(body, mesh=mesh, in_specs=in_specs, out_specs=out_specs, check_vma=False)
```

```python
import jax
import jax.numpy as jnp
from jax import lax
from jax.sharding import PartitionSpec as P

W = 8
PRIMAL = 8
ITERS = 2


SHIFT = 0.06
TRANSFORM_PRECISION = lax.Precision.HIGH
KAPPA = 1.0


def with_halo(block, sides, width):
    for axis, dim in sides:
        count = lax.axis_size(axis)
        forward = [(i, i + 1) for i in range(count - 1)]
        backward = [(target, source) for source, target in forward]
        low = lax.ppermute(
            lax.slice_in_dim(block, block.shape[dim] - width, None, axis=dim), axis, forward
        )
        high = lax.ppermute(lax.slice_in_dim(block, 0, width, axis=dim), axis, backward)
        block = jnp.concatenate([low, block, high], axis=dim)
    return block


def passed_along(block, axis, distance):
    devices = range(lax.axis_size(axis))
    route = [(i - distance, i) for i in devices if i - distance in devices]
    return lax.ppermute(block, axis, route)


def tree_sum(values):
    while len(values) > 1:
        values = [values[i] + values[i + 1] for i in range(0, len(values), 2)]
    return values[0]


def total_over(value, axes=("wide", "narrow"), radix=4):
    for axis in axes:
        count = lax.axis_size(axis)
        stride = 1
        while stride < count:
            width = min(radix, count // stride)
            pulled = [
                lax.ppermute(value, axis, [(i, i ^ (j * stride)) for i in range(count)])
                for j in range(1, width)
            ]
            value = tree_sum([value] + pulled)
            stride *= width
    return value


def sine_basis(extent):
    indices = jnp.arange(extent, dtype=jnp.float32) + 1.0
    angles = jnp.pi * indices[:, None] * indices[None, :] / (extent + 1)
    sine_table = jnp.sqrt(2.0 / (extent + 1)) * jnp.sin(angles)
    eigenvalues = 2.0 - 2.0 * jnp.cos(jnp.pi * indices / (extent + 1))
    return (sine_table, eigenvalues)


def harmonic(first, second):
    return 2.0 * first * second / (first + second)


def face_weights(padded_cond, conductance):
    face_x = harmonic(padded_cond[:-1, 1:-1], padded_cond[1:, 1:-1])
    face_y = harmonic(padded_cond[1:-1, :-1], padded_cond[1:-1, 1:])
    face_z = harmonic(conductance[:, :, :-1], conductance[:, :, 1:])
    return (face_x, face_y, face_z)


def operate(field, padded_field, reaction, face_x, face_y, face_z):
    result = reaction * field
    result = (
        result
        + face_x[1:] * (field - padded_field[2:, 1:-1])
        + face_x[:-1] * (field - padded_field[:-2, 1:-1])
    )
    result = (
        result
        + face_y[:, 1:] * (field - padded_field[1:-1, 2:])
        + face_y[:, :-1] * (field - padded_field[1:-1, :-2])
    )
    flux_z = face_z * (field[:, :, :-1] - field[:, :, 1:])
    return (
        result
        + jnp.pad(flux_z, ((0, 0), (0, 0), (0, 1)))
        - jnp.pad(flux_z, ((0, 0), (0, 0), (1, 0)))
    )


def transform_first(field, table_x):
    return jnp.einsum("ryz,re->eyz", field, table_x, precision=TRANSFORM_PRECISION)


def transform_cross(field, table_y, table_z):
    inner = jnp.einsum("ryz,zc->ryc", field, table_z, precision=TRANSFORM_PRECISION)
    return jnp.einsum("ryc,yb->rbc", inner, table_y, precision=TRANSFORM_PRECISION)


def body(source, reaction, conductance, coarse_inverse):
    block_x, block_y, block_z = source.shape
    extended = block_x + 2 * W
    padded_cond = with_halo(conductance, (("wide", 0), ("narrow", 1)), 1)
    face_x, face_y, face_z = face_weights(padded_cond, conductance)
    table_x, eigen_x = sine_basis(extended)
    table_y, eigen_y = sine_basis(block_y)
    table_z, eigen_z = sine_basis(block_z)
    spectrum = SHIFT + KAPPA * (
        eigen_x[:, None, None] + eigen_y[None, :, None] + eigen_z[None, None, :]
    )
    coarse_rows = coarse_inverse.reshape(PRIMAL, -1)

    def widen(field):
        return with_halo(field, (("wide", 0),), W)

    def fold_back(solved):
        owned = solved[W : W + block_x]
        for offset in (1, -1):
            rim_piece = solved[W + block_x :] if offset == 1 else solved[:W]
            arrived = passed_along(rim_piece, "wide", offset)
            if offset == 1:
                owned = owned + jnp.pad(arrived, ((0, block_x - W), (0, 0), (0, 0)))
            else:
                owned = owned + jnp.pad(arrived, ((block_x - W, 0), (0, 0), (0, 0)))
        return owned

    slot = lax.axis_index("wide") * lax.axis_size("narrow") + lax.axis_index("narrow")

    def placed_means(field):
        along_x = field.reshape(2, block_x // 2, block_y, block_z).sum(axis=1)
        along_y = along_x.reshape(2, 2, block_y // 2, block_z).sum(axis=2)
        along_z = along_y.reshape(2, 2, 2, block_z // 2).sum(axis=3)
        octant_means = (along_z / ((block_x // 2) * (block_y // 2) * (block_z // 2))).reshape(PRIMAL)
        return lax.dynamic_update_slice(
            jnp.zeros((coarse_rows.shape[1],), octant_means.dtype), octant_means, (slot * PRIMAL,)
        )

    def precondition(field, all_means):
        coeffs = transform_first(widen(transform_cross(field, table_y, table_z)), table_x) / spectrum
        local_part = transform_cross(fold_back(transform_first(coeffs, table_x)), table_y, table_z)
        correction = jnp.dot(coarse_rows, all_means, precision=lax.Precision.HIGHEST).reshape(
            2, 2, 2
        )
        upper_z = lax.broadcasted_iota(jnp.int32, (1, 1, block_z), 2) >= block_z // 2
        rows = jnp.where(upper_z, correction[:, :, 1:2], correction[:, :, 0:1])
        spread = jnp.broadcast_to(
            rows[:, None, :, None, :], (2, block_x // 2, 2, block_y // 2, block_z)
        )
        return local_part + spread.reshape(block_x, block_y, block_z)

    def apply_matrix(field):
        padded_field = with_halo(field, (("wide", 0), ("narrow", 1)), 1)
        return operate(field, padded_field, reaction, face_x, face_y, face_z)

    residual = source
    residual_means = total_over(placed_means(residual))
    preconditioned = precondition(residual, residual_means)
    bent = apply_matrix(preconditioned)
    sums = total_over(
        jnp.concatenate(
            [
                jnp.stack([jnp.sum(residual * preconditioned), jnp.sum(preconditioned * bent)]),
                placed_means(bent),
            ]
        )
    )
    gamma_now, curvature, image_means = sums[0], sums[1], sums[2:]
    direction, image = preconditioned, bent
    step_size = gamma_now / curvature
    solution = step_size * direction
    residual = residual - step_size * image
    residual_means = residual_means - step_size * image_means
    for iteration in range(1, ITERS):
        preconditioned = precondition(residual, residual_means)
        bent = apply_matrix(preconditioned)
        sums = total_over(
            jnp.concatenate(
                [
                    jnp.stack(
                        [
                            jnp.sum(residual * preconditioned),
                            jnp.sum(preconditioned * bent),
                            jnp.sum(preconditioned * image),
                            jnp.sum(direction * bent),
                        ]
                    ),
                    placed_means(bent),
                ]
            )
        )
        gamma_next = sums[0]
        ratio = gamma_next / gamma_now
        curvature = sums[1] + ratio * (sums[2] + sums[3]) + ratio * ratio * curvature
        direction = preconditioned + ratio * direction
        image = bent + ratio * image
        image_means = sums[4:] + ratio * image_means
        gamma_now = gamma_next
        step_size = gamma_now / curvature
        solution = solution + step_size * direction
        residual = residual - step_size * image
        residual_means = residual_means - step_size * image_means
    preconditioned = precondition(residual, residual_means)
    gamma_next = total_over(jnp.sum(residual * preconditioned))
    direction = preconditioned + gamma_next / gamma_now * direction
    return (solution, residual, direction)


def solution(mesh):
    in_specs = (
        P("wide", "narrow", None),
        P("wide", "narrow", None),
        P("wide", "narrow", None),
        P("wide", "narrow", None, None),
    )
    out_specs = (P("wide", "narrow", None), P("wide", "narrow", None), P("wide", "narrow", None))
    return jax.shard_map(body, mesh=mesh, in_specs=in_specs, out_specs=out_specs, check_vma=False)
```

```python
import jax
import jax.numpy as jnp
from jax import lax
from jax.sharding import PartitionSpec as P

W = 8
PRIMAL = 8
ITERS = 2


SHIFT = 0.06
TRANSFORM_PRECISION = lax.Precision.HIGH
KAPPA = 1.0


def with_halo(block, sides, width):
    for axis, dim in sides:
        count = lax.axis_size(axis)
        forward = [(i, i + 1) for i in range(count - 1)]
        backward = [(target, source) for source, target in forward]
        low = lax.ppermute(
            lax.slice_in_dim(block, block.shape[dim] - width, None, axis=dim), axis, forward
        )
        high = lax.ppermute(lax.slice_in_dim(block, 0, width, axis=dim), axis, backward)
        block = jnp.concatenate([low, block, high], axis=dim)
    return block


def passed_along(block, axis, distance):
    devices = range(lax.axis_size(axis))
    route = [(i - distance, i) for i in devices if i - distance in devices]
    return lax.ppermute(block, axis, route)


def tree_sum(values):
    while len(values) > 1:
        values = [values[i] + values[i + 1] for i in range(0, len(values), 2)]
    return values[0]


def total_over(value, axes=("wide", "narrow"), radix=4):
    for axis in axes:
        count = lax.axis_size(axis)
        stride = 1
        while stride < count:
            width = min(radix, count // stride)
            pulled = [
                lax.ppermute(value, axis, [(i, i ^ (j * stride)) for i in range(count)])
                for j in range(1, width)
            ]
            value = tree_sum([value] + pulled)
            stride *= width
    return value


def sine_basis(extent):
    indices = jnp.arange(extent, dtype=jnp.float32) + 1.0
    angles = jnp.pi * indices[:, None] * indices[None, :] / (extent + 1)
    sine_table = jnp.sqrt(2.0 / (extent + 1)) * jnp.sin(angles)
    eigenvalues = 2.0 - 2.0 * jnp.cos(jnp.pi * indices / (extent + 1))
    return (sine_table, eigenvalues)


def harmonic(first, second):
    return 2.0 * first * second / (first + second)


def face_weights(padded_cond, conductance):
    face_x = harmonic(padded_cond[:-1, 1:-1], padded_cond[1:, 1:-1])
    face_y = harmonic(padded_cond[1:-1, :-1], padded_cond[1:-1, 1:])
    face_z = harmonic(conductance[:, :, :-1], conductance[:, :, 1:])
    return (face_x, face_y, face_z)


def operate(field, padded_field, reaction, face_x, face_y, face_z):
    result = reaction * field
    result = (
        result
        + face_x[1:] * (field - padded_field[2:, 1:-1])
        + face_x[:-1] * (field - padded_field[:-2, 1:-1])
    )
    result = (
        result
        + face_y[:, 1:] * (field - padded_field[1:-1, 2:])
        + face_y[:, :-1] * (field - padded_field[1:-1, :-2])
    )
    flux_z = face_z * (field[:, :, :-1] - field[:, :, 1:])
    return (
        result
        + jnp.pad(flux_z, ((0, 0), (0, 0), (0, 1)))
        - jnp.pad(flux_z, ((0, 0), (0, 0), (1, 0)))
    )


def transform_first(field, table_x):
    return jnp.einsum("ryz,re->eyz", field, table_x, precision=TRANSFORM_PRECISION)


def transform_cross(field, table_y, table_z):
    inner = jnp.einsum("ryz,zc->ryc", field, table_z, precision=TRANSFORM_PRECISION)
    return jnp.einsum("ryc,yb->rbc", inner, table_y, precision=TRANSFORM_PRECISION)


def body(source, reaction, conductance, coarse_inverse):
    block_x, block_y, block_z = source.shape
    extended = block_x + 2 * W
    table_x, eigen_x = sine_basis(extended)
    table_y, eigen_y = sine_basis(block_y)
    table_z, eigen_z = sine_basis(block_z)
    spectrum = SHIFT + KAPPA * (
        eigen_x[:, None, None] + eigen_y[None, :, None] + eigen_z[None, None, :]
    )
    coarse_rows = coarse_inverse.reshape(PRIMAL, -1)
    first_rows = transform_cross(source, table_y, table_z)
    wide_count = lax.axis_size("wide")
    forward = [(i, i + 1) for i in range(wide_count - 1)]
    backward = [(target, origin) for origin, target in forward]
    low = lax.ppermute(
        jnp.concatenate([first_rows[block_x - W :], conductance[block_x - 1 :]], axis=0),
        "wide",
        forward,
    )
    high = lax.ppermute(
        jnp.concatenate([first_rows[:W], conductance[:1]], axis=0), "wide", backward
    )
    first_extended = jnp.concatenate([low[:W], first_rows, high[:W]], axis=0)
    padded_cond = with_halo(
        jnp.concatenate([low[W:], conductance, high[W:]], axis=0), (("narrow", 1),), 1
    )
    face_x, face_y, face_z = face_weights(padded_cond, conductance)

    def widen(field):
        return with_halo(field, (("wide", 0),), W)

    def fold_back(solved):
        owned = solved[W : W + block_x]
        for offset in (1, -1):
            rim_piece = solved[W + block_x :] if offset == 1 else solved[:W]
            arrived = passed_along(rim_piece, "wide", offset)
            if offset == 1:
                owned = owned + jnp.pad(arrived, ((0, block_x - W), (0, 0), (0, 0)))
            else:
                owned = owned + jnp.pad(arrived, ((block_x - W, 0), (0, 0), (0, 0)))
        return owned

    slot = lax.axis_index("wide") * lax.axis_size("narrow") + lax.axis_index("narrow")

    def placed_means(field):
        along_x = field.reshape(2, block_x // 2, block_y, block_z).sum(axis=1)
        along_y = along_x.reshape(2, 2, block_y // 2, block_z).sum(axis=2)
        along_z = along_y.reshape(2, 2, 2, block_z // 2).sum(axis=3)
        octant_means = (along_z / ((block_x // 2) * (block_y // 2) * (block_z // 2))).reshape(PRIMAL)
        return lax.dynamic_update_slice(
            jnp.zeros((coarse_rows.shape[1],), octant_means.dtype), octant_means, (slot * PRIMAL,)
        )

    def precondition(field, all_means, extended=None):
        if extended is None:
            extended = widen(transform_cross(field, table_y, table_z))
        coeffs = transform_first(extended, table_x) / spectrum
        local_part = transform_cross(fold_back(transform_first(coeffs, table_x)), table_y, table_z)
        correction = jnp.dot(coarse_rows, all_means, precision=lax.Precision.HIGHEST).reshape(
            2, 2, 2
        )
        upper_z = lax.broadcasted_iota(jnp.int32, (1, 1, block_z), 2) >= block_z // 2
        rows = jnp.where(upper_z, correction[:, :, 1:2], correction[:, :, 0:1])
        spread = jnp.broadcast_to(
            rows[:, None, :, None, :], (2, block_x // 2, 2, block_y // 2, block_z)
        )
        return local_part + spread.reshape(block_x, block_y, block_z)

    def apply_matrix(field):
        padded_field = with_halo(field, (("wide", 0), ("narrow", 1)), 1)
        return operate(field, padded_field, reaction, face_x, face_y, face_z)

    residual = source
    residual_means = total_over(placed_means(residual))
    preconditioned = precondition(residual, residual_means, first_extended)
    bent = apply_matrix(preconditioned)
    sums = total_over(
        jnp.concatenate(
            [
                jnp.stack([jnp.sum(residual * preconditioned), jnp.sum(preconditioned * bent)]),
                placed_means(bent),
            ]
        )
    )
    gamma_now, curvature, image_means = sums[0], sums[1], sums[2:]
    direction, image = preconditioned, bent
    step_size = gamma_now / curvature
    solution = step_size * direction
    residual = residual - step_size * image
    residual_means = residual_means - step_size * image_means
    for iteration in range(1, ITERS):
        preconditioned = precondition(residual, residual_means)
        bent = apply_matrix(preconditioned)
        sums = total_over(
            jnp.concatenate(
                [
                    jnp.stack(
                        [
                            jnp.sum(residual * preconditioned),
                            jnp.sum(preconditioned * bent),
                            jnp.sum(preconditioned * image),
                            jnp.sum(direction * bent),
                        ]
                    ),
                    placed_means(bent),
                ]
            )
        )
        gamma_next = sums[0]
        ratio = gamma_next / gamma_now
        curvature = sums[1] + ratio * (sums[2] + sums[3]) + ratio * ratio * curvature
        direction = preconditioned + ratio * direction
        image = bent + ratio * image
        image_means = sums[4:] + ratio * image_means
        gamma_now = gamma_next
        step_size = gamma_now / curvature
        solution = solution + step_size * direction
        residual = residual - step_size * image
        residual_means = residual_means - step_size * image_means
    preconditioned = precondition(residual, residual_means)
    gamma_next = total_over(jnp.sum(residual * preconditioned))
    direction = preconditioned + gamma_next / gamma_now * direction
    return (solution, residual, direction)


def solution(mesh):
    in_specs = (
        P("wide", "narrow", None),
        P("wide", "narrow", None),
        P("wide", "narrow", None),
        P("wide", "narrow", None, None),
    )
    out_specs = (P("wide", "narrow", None), P("wide", "narrow", None), P("wide", "narrow", None))
    return jax.shard_map(body, mesh=mesh, in_specs=in_specs, out_specs=out_specs, check_vma=False)
```

```python
import jax
import jax.numpy as jnp
from jax import lax
from jax.sharding import PartitionSpec as P

W = 8
PRIMAL = 8
ITERS = 2


SHIFT = 0.06
TRANSFORM_PRECISION = lax.Precision.HIGH
KAPPA = 1.0


def with_halo(block, sides, width):
    for axis, dim in sides:
        count = lax.axis_size(axis)
        forward = [(i, i + 1) for i in range(count - 1)]
        backward = [(target, source) for source, target in forward]
        low = lax.ppermute(
            lax.slice_in_dim(block, block.shape[dim] - width, None, axis=dim), axis, forward
        )
        high = lax.ppermute(lax.slice_in_dim(block, 0, width, axis=dim), axis, backward)
        block = jnp.concatenate([low, block, high], axis=dim)
    return block


def with_cross_halo(block):
    pieces = []
    for axis, dim in (("wide", 0), ("narrow", 1)):
        count = lax.axis_size(axis)
        forward = [(i, i + 1) for i in range(count - 1)]
        backward = [(target, source) for source, target in forward]
        low = lax.ppermute(
            lax.slice_in_dim(block, block.shape[dim] - 1, None, axis=dim), axis, forward
        )
        high = lax.ppermute(lax.slice_in_dim(block, 0, 1, axis=dim), axis, backward)
        pieces.append((low, high))
    (top, bottom), (left, right) = pieces
    corner = jnp.zeros((1, 1, block.shape[2]), block.dtype)
    middle = jnp.concatenate([left, block, right], axis=1)
    top = jnp.concatenate([corner, top, corner], axis=1)
    bottom = jnp.concatenate([corner, bottom, corner], axis=1)
    return jnp.concatenate([top, middle, bottom], axis=0)


def passed_along(block, axis, distance):
    devices = range(lax.axis_size(axis))
    route = [(i - distance, i) for i in devices if i - distance in devices]
    return lax.ppermute(block, axis, route)


def tree_sum(values):
    while len(values) > 1:
        values = [values[i] + values[i + 1] for i in range(0, len(values), 2)]
    return values[0]


def total_over(value, axes=("wide", "narrow"), radix=4):
    for axis in axes:
        count = lax.axis_size(axis)
        stride = 1
        while stride < count:
            width = min(radix, count // stride)
            pulled = [
                lax.ppermute(value, axis, [(i, i ^ (j * stride)) for i in range(count)])
                for j in range(1, width)
            ]
            value = tree_sum([value] + pulled)
            stride *= width
    return value


def sine_basis(extent):
    indices = jnp.arange(extent, dtype=jnp.float32) + 1.0
    angles = jnp.pi * indices[:, None] * indices[None, :] / (extent + 1)
    sine_table = jnp.sqrt(2.0 / (extent + 1)) * jnp.sin(angles)
    eigenvalues = 2.0 - 2.0 * jnp.cos(jnp.pi * indices / (extent + 1))
    return (sine_table, eigenvalues)


def harmonic(first, second):
    return 2.0 * first * second / (first + second)


def face_weights(padded_cond, conductance):
    face_x = harmonic(padded_cond[:-1, 1:-1], padded_cond[1:, 1:-1])
    face_y = harmonic(padded_cond[1:-1, :-1], padded_cond[1:-1, 1:])
    face_z = harmonic(conductance[:, :, :-1], conductance[:, :, 1:])
    return (face_x, face_y, face_z)


def operate(field, padded_field, reaction, face_x, face_y, face_z):
    result = reaction * field
    result = (
        result
        + face_x[1:] * (field - padded_field[2:, 1:-1])
        + face_x[:-1] * (field - padded_field[:-2, 1:-1])
    )
    result = (
        result
        + face_y[:, 1:] * (field - padded_field[1:-1, 2:])
        + face_y[:, :-1] * (field - padded_field[1:-1, :-2])
    )
    flux_z = face_z * (field[:, :, :-1] - field[:, :, 1:])
    return (
        result
        + jnp.pad(flux_z, ((0, 0), (0, 0), (0, 1)))
        - jnp.pad(flux_z, ((0, 0), (0, 0), (1, 0)))
    )


def transform_first(field, table_x):
    return jnp.einsum("ryz,re->eyz", field, table_x, precision=TRANSFORM_PRECISION)


def transform_cross(field, table_y, table_z):
    inner = jnp.einsum("ryz,zc->ryc", field, table_z, precision=TRANSFORM_PRECISION)
    return jnp.einsum("ryc,yb->rbc", inner, table_y, precision=TRANSFORM_PRECISION)


def body(source, reaction, conductance, coarse_inverse):
    block_x, block_y, block_z = source.shape
    extended = block_x + 2 * W
    table_x, eigen_x = sine_basis(extended)
    table_y, eigen_y = sine_basis(block_y)
    table_z, eigen_z = sine_basis(block_z)
    spectrum = SHIFT + KAPPA * (
        eigen_x[:, None, None] + eigen_y[None, :, None] + eigen_z[None, None, :]
    )
    coarse_rows = coarse_inverse.reshape(PRIMAL, -1)
    first_rows = transform_cross(source, table_y, table_z)
    wide_count = lax.axis_size("wide")
    forward = [(i, i + 1) for i in range(wide_count - 1)]
    backward = [(target, origin) for origin, target in forward]
    low = lax.ppermute(
        jnp.concatenate([first_rows[block_x - W :], conductance[block_x - 1 :]], axis=0),
        "wide",
        forward,
    )
    high = lax.ppermute(
        jnp.concatenate([first_rows[:W], conductance[:1]], axis=0), "wide", backward
    )
    first_extended = jnp.concatenate([low[:W], first_rows, high[:W]], axis=0)
    padded_cond = with_halo(
        jnp.concatenate([low[W:], conductance, high[W:]], axis=0), (("narrow", 1),), 1
    )
    face_x, face_y, face_z = face_weights(padded_cond, conductance)

    def widen(field):
        return with_halo(field, (("wide", 0),), W)

    def fold_back(solved):
        owned = solved[W : W + block_x]
        for offset in (1, -1):
            rim_piece = solved[W + block_x :] if offset == 1 else solved[:W]
            arrived = passed_along(rim_piece, "wide", offset)
            if offset == 1:
                owned = owned + jnp.pad(arrived, ((0, block_x - W), (0, 0), (0, 0)))
            else:
                owned = owned + jnp.pad(arrived, ((block_x - W, 0), (0, 0), (0, 0)))
        return owned

    slot = lax.axis_index("wide") * lax.axis_size("narrow") + lax.axis_index("narrow")

    def placed_means(field):
        along_x = field.reshape(2, block_x // 2, block_y, block_z).sum(axis=1)
        along_y = along_x.reshape(2, 2, block_y // 2, block_z).sum(axis=2)
        along_z = along_y.reshape(2, 2, 2, block_z // 2).sum(axis=3)
        octant_means = (along_z / ((block_x // 2) * (block_y // 2) * (block_z // 2))).reshape(PRIMAL)
        return lax.dynamic_update_slice(
            jnp.zeros((coarse_rows.shape[1],), octant_means.dtype), octant_means, (slot * PRIMAL,)
        )

    def precondition(field, all_means, extended=None):
        if extended is None:
            extended = widen(transform_cross(field, table_y, table_z))
        coeffs = transform_first(extended, table_x) / spectrum
        local_part = transform_cross(fold_back(transform_first(coeffs, table_x)), table_y, table_z)
        correction = jnp.dot(coarse_rows, all_means, precision=lax.Precision.HIGHEST).reshape(
            2, 2, 2
        )
        upper_z = lax.broadcasted_iota(jnp.int32, (1, 1, block_z), 2) >= block_z // 2
        rows = jnp.where(upper_z, correction[:, :, 1:2], correction[:, :, 0:1])
        spread = jnp.broadcast_to(
            rows[:, None, :, None, :], (2, block_x // 2, 2, block_y // 2, block_z)
        )
        return local_part + spread.reshape(block_x, block_y, block_z)

    def apply_matrix(field):
        padded_field = with_cross_halo(field)
        return operate(field, padded_field, reaction, face_x, face_y, face_z)

    residual = source
    residual_means = total_over(placed_means(residual))
    preconditioned = precondition(residual, residual_means, first_extended)
    bent = apply_matrix(preconditioned)
    sums = total_over(
        jnp.concatenate(
            [
                jnp.stack([jnp.sum(residual * preconditioned), jnp.sum(preconditioned * bent)]),
                placed_means(bent),
            ]
        )
    )
    gamma_now, curvature, image_means = sums[0], sums[1], sums[2:]
    direction, image = preconditioned, bent
    step_size = gamma_now / curvature
    solution = step_size * direction
    residual = residual - step_size * image
    residual_means = residual_means - step_size * image_means
    for iteration in range(1, ITERS):
        preconditioned = precondition(residual, residual_means)
        bent = apply_matrix(preconditioned)
        sums = total_over(
            jnp.concatenate(
                [
                    jnp.stack(
                        [
                            jnp.sum(residual * preconditioned),
                            jnp.sum(preconditioned * bent),
                            jnp.sum(preconditioned * image),
                            jnp.sum(direction * bent),
                        ]
                    ),
                    placed_means(bent),
                ]
            )
        )
        gamma_next = sums[0]
        ratio = gamma_next / gamma_now
        curvature = sums[1] + ratio * (sums[2] + sums[3]) + ratio * ratio * curvature
        direction = preconditioned + ratio * direction
        image = bent + ratio * image
        image_means = sums[4:] + ratio * image_means
        gamma_now = gamma_next
        step_size = gamma_now / curvature
        solution = solution + step_size * direction
        residual = residual - step_size * image
        residual_means = residual_means - step_size * image_means
    preconditioned = precondition(residual, residual_means)
    gamma_next = total_over(jnp.sum(residual * preconditioned))
    direction = preconditioned + gamma_next / gamma_now * direction
    return (solution, residual, direction)


def solution(mesh):
    in_specs = (
        P("wide", "narrow", None),
        P("wide", "narrow", None),
        P("wide", "narrow", None),
        P("wide", "narrow", None, None),
    )
    out_specs = (P("wide", "narrow", None), P("wide", "narrow", None), P("wide", "narrow", None))
    return jax.shard_map(body, mesh=mesh, in_specs=in_specs, out_specs=out_specs, check_vma=False)
```

```python
import jax
import jax.numpy as jnp
from jax import lax
from jax.sharding import PartitionSpec as P

W = 8
PRIMAL = 8
ITERS = 2


SHIFT = 0.06
TRANSFORM_PRECISION = lax.Precision.HIGHEST
KAPPA = 1.0


def with_halo(block, sides, width):
    for axis, dim in sides:
        count = lax.axis_size(axis)
        forward = [(i, i + 1) for i in range(count - 1)]
        backward = [(target, source) for source, target in forward]
        low = lax.ppermute(
            lax.slice_in_dim(block, block.shape[dim] - width, None, axis=dim), axis, forward
        )
        high = lax.ppermute(lax.slice_in_dim(block, 0, width, axis=dim), axis, backward)
        block = jnp.concatenate([low, block, high], axis=dim)
    return block


def with_cross_halo(block):
    pieces = []
    for axis, dim in (("wide", 0), ("narrow", 1)):
        count = lax.axis_size(axis)
        forward = [(i, i + 1) for i in range(count - 1)]
        backward = [(target, source) for source, target in forward]
        low = lax.ppermute(
            lax.slice_in_dim(block, block.shape[dim] - 1, None, axis=dim), axis, forward
        )
        high = lax.ppermute(lax.slice_in_dim(block, 0, 1, axis=dim), axis, backward)
        pieces.append((low, high))
    (top, bottom), (left, right) = pieces
    corner = jnp.zeros((1, 1, block.shape[2]), block.dtype)
    middle = jnp.concatenate([left, block, right], axis=1)
    top = jnp.concatenate([corner, top, corner], axis=1)
    bottom = jnp.concatenate([corner, bottom, corner], axis=1)
    return jnp.concatenate([top, middle, bottom], axis=0)


def passed_along(block, axis, distance):
    devices = range(lax.axis_size(axis))
    route = [(i - distance, i) for i in devices if i - distance in devices]
    return lax.ppermute(block, axis, route)


def tree_sum(values):
    while len(values) > 1:
        values = [values[i] + values[i + 1] for i in range(0, len(values), 2)]
    return values[0]


def total_over(value, axes=("wide", "narrow"), radix=4):
    for axis in axes:
        count = lax.axis_size(axis)
        stride = 1
        while stride < count:
            width = min(radix, count // stride)
            pulled = [
                lax.ppermute(value, axis, [(i, i ^ (j * stride)) for i in range(count)])
                for j in range(1, width)
            ]
            value = tree_sum([value] + pulled)
            stride *= width
    return value


def sine_basis(extent):
    indices = jnp.arange(extent, dtype=jnp.float32) + 1.0
    angles = jnp.pi * indices[:, None] * indices[None, :] / (extent + 1)
    sine_table = jnp.sqrt(2.0 / (extent + 1)) * jnp.sin(angles)
    eigenvalues = 2.0 - 2.0 * jnp.cos(jnp.pi * indices / (extent + 1))
    return (sine_table, eigenvalues)


def harmonic(first, second):
    return 2.0 * first * second / (first + second)


def face_weights(padded_cond, conductance):
    face_x = harmonic(padded_cond[:-1, 1:-1], padded_cond[1:, 1:-1])
    face_y = harmonic(padded_cond[1:-1, :-1], padded_cond[1:-1, 1:])
    face_z = harmonic(conductance[:, :, :-1], conductance[:, :, 1:])
    return (face_x, face_y, face_z)


def operate(field, padded_field, reaction, face_x, face_y, face_z):
    result = reaction * field
    result = (
        result
        + face_x[1:] * (field - padded_field[2:, 1:-1])
        + face_x[:-1] * (field - padded_field[:-2, 1:-1])
    )
    result = (
        result
        + face_y[:, 1:] * (field - padded_field[1:-1, 2:])
        + face_y[:, :-1] * (field - padded_field[1:-1, :-2])
    )
    flux_z = face_z * (field[:, :, :-1] - field[:, :, 1:])
    return (
        result
        + jnp.pad(flux_z, ((0, 0), (0, 0), (0, 1)))
        - jnp.pad(flux_z, ((0, 0), (0, 0), (1, 0)))
    )


def transform_first(field, table_x):
    return jnp.einsum("ryz,re->eyz", field, table_x, precision=TRANSFORM_PRECISION)


def transform_cross(field, table_y, table_z):
    inner = jnp.einsum("ryz,zc->ryc", field, table_z, precision=TRANSFORM_PRECISION)
    return jnp.einsum("ryc,yb->rbc", inner, table_y, precision=TRANSFORM_PRECISION)


def body(source, reaction, conductance, coarse_inverse):
    block_x, block_y, block_z = source.shape
    extended = block_x + 2 * W
    table_x, eigen_x = sine_basis(extended)
    table_y, eigen_y = sine_basis(block_y)
    table_z, eigen_z = sine_basis(block_z)
    spectrum = SHIFT + KAPPA * (
        eigen_x[:, None, None] + eigen_y[None, :, None] + eigen_z[None, None, :]
    )
    coarse_rows = coarse_inverse.reshape(PRIMAL, -1)
    first_rows = transform_cross(source, table_y, table_z)
    wide_count = lax.axis_size("wide")
    forward = [(i, i + 1) for i in range(wide_count - 1)]
    backward = [(target, origin) for origin, target in forward]
    low = lax.ppermute(
        jnp.concatenate([first_rows[block_x - W :], conductance[block_x - 1 :]], axis=0),
        "wide",
        forward,
    )
    high = lax.ppermute(
        jnp.concatenate([first_rows[:W], conductance[:1]], axis=0), "wide", backward
    )
    first_extended = jnp.concatenate([low[:W], first_rows, high[:W]], axis=0)
    padded_cond = with_halo(
        jnp.concatenate([low[W:], conductance, high[W:]], axis=0), (("narrow", 1),), 1
    )
    face_x, face_y, face_z = face_weights(padded_cond, conductance)

    def widen(field):
        return with_halo(field, (("wide", 0),), W)

    def fold_back(solved):
        owned = solved[W : W + block_x]
        for offset in (1, -1):
            rim_piece = solved[W + block_x :] if offset == 1 else solved[:W]
            arrived = passed_along(rim_piece, "wide", offset)
            if offset == 1:
                owned = owned + jnp.pad(arrived, ((0, block_x - W), (0, 0), (0, 0)))
            else:
                owned = owned + jnp.pad(arrived, ((block_x - W, 0), (0, 0), (0, 0)))
        return owned

    slot = lax.axis_index("wide") * lax.axis_size("narrow") + lax.axis_index("narrow")

    def placed_means(field):
        along_x = field.reshape(2, block_x // 2, block_y, block_z).sum(axis=1)
        along_y = along_x.reshape(2, 2, block_y // 2, block_z).sum(axis=2)
        along_z = along_y.reshape(2, 2, 2, block_z // 2).sum(axis=3)
        octant_means = (along_z / ((block_x // 2) * (block_y // 2) * (block_z // 2))).reshape(PRIMAL)
        return lax.dynamic_update_slice(
            jnp.zeros((coarse_rows.shape[1],), octant_means.dtype), octant_means, (slot * PRIMAL,)
        )

    def precondition(field, all_means, extended=None):
        if extended is None:
            extended = widen(transform_cross(field, table_y, table_z))
        coeffs = transform_first(extended, table_x) / spectrum
        local_part = transform_cross(fold_back(transform_first(coeffs, table_x)), table_y, table_z)
        correction = jnp.dot(coarse_rows, all_means, precision=lax.Precision.HIGHEST).reshape(
            2, 2, 2
        )
        upper_z = lax.broadcasted_iota(jnp.int32, (1, 1, block_z), 2) >= block_z // 2
        rows = jnp.where(upper_z, correction[:, :, 1:2], correction[:, :, 0:1])
        spread = jnp.broadcast_to(
            rows[:, None, :, None, :], (2, block_x // 2, 2, block_y // 2, block_z)
        )
        return local_part + spread.reshape(block_x, block_y, block_z)

    def apply_matrix(field):
        padded_field = with_cross_halo(field)
        return operate(field, padded_field, reaction, face_x, face_y, face_z)

    residual = source
    residual_means = total_over(placed_means(residual))
    preconditioned = precondition(residual, residual_means, first_extended)
    bent = apply_matrix(preconditioned)
    sums = total_over(
        jnp.concatenate(
            [
                jnp.stack([jnp.sum(residual * preconditioned), jnp.sum(preconditioned * bent)]),
                placed_means(bent),
            ]
        )
    )
    gamma_now, curvature, image_means = sums[0], sums[1], sums[2:]
    direction, image = preconditioned, bent
    step_size = gamma_now / curvature
    solution = step_size * direction
    residual = residual - step_size * image
    residual_means = residual_means - step_size * image_means
    for iteration in range(1, ITERS):
        preconditioned = precondition(residual, residual_means)
        bent = apply_matrix(preconditioned)
        sums = total_over(
            jnp.concatenate(
                [
                    jnp.stack(
                        [
                            jnp.sum(residual * preconditioned),
                            jnp.sum(preconditioned * bent),
                            jnp.sum(preconditioned * image),
                            jnp.sum(direction * bent),
                        ]
                    ),
                    placed_means(bent),
                ]
            )
        )
        gamma_next = sums[0]
        ratio = gamma_next / gamma_now
        curvature = sums[1] + ratio * (sums[2] + sums[3]) + ratio * ratio * curvature
        direction = preconditioned + ratio * direction
        image = bent + ratio * image
        image_means = sums[4:] + ratio * image_means
        gamma_now = gamma_next
        step_size = gamma_now / curvature
        solution = solution + step_size * direction
        residual = residual - step_size * image
        residual_means = residual_means - step_size * image_means
    preconditioned = precondition(residual, residual_means)
    gamma_next = total_over(jnp.sum(residual * preconditioned))
    direction = preconditioned + gamma_next / gamma_now * direction
    return (solution, residual, direction)


def solution(mesh):
    in_specs = (
        P("wide", "narrow", None),
        P("wide", "narrow", None),
        P("wide", "narrow", None),
        P("wide", "narrow", None, None),
    )
    out_specs = (P("wide", "narrow", None), P("wide", "narrow", None), P("wide", "narrow", None))
    return jax.shard_map(body, mesh=mesh, in_specs=in_specs, out_specs=out_specs, check_vma=False)
```

```python
import jax
import jax.numpy as jnp
from jax import lax
from jax.sharding import PartitionSpec as P

W = 8
PRIMAL = 8
ITERS = 2


SHIFT = 0.06
TRANSFORM_PRECISION = lax.Precision.HIGH
KAPPA = 1.0


def with_halo(block, sides, width):
    for axis, dim in sides:
        count = lax.axis_size(axis)
        forward = [(i, i + 1) for i in range(count - 1)]
        backward = [(target, source) for source, target in forward]
        low = lax.ppermute(
            lax.slice_in_dim(block, block.shape[dim] - width, None, axis=dim), axis, forward
        )
        high = lax.ppermute(lax.slice_in_dim(block, 0, width, axis=dim), axis, backward)
        block = jnp.concatenate([low, block, high], axis=dim)
    return block


def with_cross_halo(block):
    pieces = []
    for axis, dim in (("wide", 0), ("narrow", 1)):
        count = lax.axis_size(axis)
        forward = [(i, i + 1) for i in range(count - 1)]
        backward = [(target, source) for source, target in forward]
        low = lax.ppermute(
            lax.slice_in_dim(block, block.shape[dim] - 1, None, axis=dim), axis, forward
        )
        high = lax.ppermute(lax.slice_in_dim(block, 0, 1, axis=dim), axis, backward)
        pieces.append((low, high))
    (top, bottom), (left, right) = pieces
    corner = jnp.zeros((1, 1, block.shape[2]), block.dtype)
    middle = jnp.concatenate([left, block, right], axis=1)
    top = jnp.concatenate([corner, top, corner], axis=1)
    bottom = jnp.concatenate([corner, bottom, corner], axis=1)
    return jnp.concatenate([top, middle, bottom], axis=0)


def passed_along(block, axis, distance):
    devices = range(lax.axis_size(axis))
    route = [(i - distance, i) for i in devices if i - distance in devices]
    return lax.ppermute(block, axis, route)


def tree_sum(values):
    while len(values) > 1:
        values = [values[i] + values[i + 1] for i in range(0, len(values), 2)]
    return values[0]


def total_over(value, axes=("wide", "narrow"), radix=4):
    for axis in axes:
        count = lax.axis_size(axis)
        stride = 1
        while stride < count:
            width = min(radix, count // stride)
            pulled = [
                lax.ppermute(value, axis, [(i, i ^ (j * stride)) for i in range(count)])
                for j in range(1, width)
            ]
            value = tree_sum([value] + pulled)
            stride *= width
    return value


def sine_basis(extent):
    indices = jnp.arange(extent, dtype=jnp.float32) + 1.0
    angles = jnp.pi * indices[:, None] * indices[None, :] / (extent + 1)
    sine_table = jnp.sqrt(2.0 / (extent + 1)) * jnp.sin(angles)
    eigenvalues = 2.0 - 2.0 * jnp.cos(jnp.pi * indices / (extent + 1))
    return (sine_table, eigenvalues)


def harmonic(first, second):
    return 2.0 * first * second / (first + second)


def face_weights(padded_cond, conductance):
    face_x = harmonic(padded_cond[:-1, 1:-1], padded_cond[1:, 1:-1])
    face_y = harmonic(padded_cond[1:-1, :-1], padded_cond[1:-1, 1:])
    face_z = harmonic(conductance[:, :, :-1], conductance[:, :, 1:])
    return (face_x, face_y, face_z)


def operate(field, padded_field, reaction, face_x, face_y, face_z):
    result = reaction * field
    result = (
        result
        + face_x[1:] * (field - padded_field[2:, 1:-1])
        + face_x[:-1] * (field - padded_field[:-2, 1:-1])
    )
    result = (
        result
        + face_y[:, 1:] * (field - padded_field[1:-1, 2:])
        + face_y[:, :-1] * (field - padded_field[1:-1, :-2])
    )
    flux_z = face_z * (field[:, :, :-1] - field[:, :, 1:])
    return (
        result
        + jnp.pad(flux_z, ((0, 0), (0, 0), (0, 1)))
        - jnp.pad(flux_z, ((0, 0), (0, 0), (1, 0)))
    )


def transform_first(field, table_x):
    return jnp.einsum("ryz,re->eyz", field, table_x, precision=TRANSFORM_PRECISION)


def transform_cross(field, table_y, table_z):
    inner = jnp.einsum("ryz,zc->ryc", field, table_z, precision=TRANSFORM_PRECISION)
    return jnp.einsum("ryc,yb->rbc", inner, table_y, precision=TRANSFORM_PRECISION)


def body(source, reaction, conductance, coarse_inverse):
    block_x, block_y, block_z = source.shape
    extended = block_x + 2 * W
    table_x, eigen_x = sine_basis(extended)
    table_y, eigen_y = sine_basis(block_y)
    table_z, eigen_z = sine_basis(block_z)
    spectrum = SHIFT + KAPPA * (
        eigen_x[:, None, None] + eigen_y[None, :, None] + eigen_z[None, None, :]
    )
    coarse_rows = coarse_inverse.reshape(PRIMAL, -1)
    first_rows = transform_cross(source, table_y, table_z)
    wide_count = lax.axis_size("wide")
    forward = [(i, i + 1) for i in range(wide_count - 1)]
    backward = [(target, origin) for origin, target in forward]
    low = lax.ppermute(
        jnp.concatenate([first_rows[block_x - W :], conductance[block_x - 1 :]], axis=0),
        "wide",
        forward,
    )
    high = lax.ppermute(
        jnp.concatenate([first_rows[:W], conductance[:1]], axis=0), "wide", backward
    )
    first_extended = jnp.concatenate([low[:W], first_rows, high[:W]], axis=0)
    narrow_count = lax.axis_size("narrow")
    ahead = [(i, i + 1) for i in range(narrow_count - 1)]
    behind = [(target, origin) for origin, target in ahead]
    left = lax.ppermute(conductance[:, block_y - 1 :], "narrow", ahead)
    right = lax.ppermute(conductance[:, :1], "narrow", behind)
    corner = jnp.zeros((1, 1, block_z), conductance.dtype)
    padded_cond = jnp.concatenate(
        [
            jnp.concatenate([corner, low[W:], corner], axis=1),
            jnp.concatenate([left, conductance, right], axis=1),
            jnp.concatenate([corner, high[W:], corner], axis=1),
        ],
        axis=0,
    )
    face_x, face_y, face_z = face_weights(padded_cond, conductance)

    def widen(field):
        return with_halo(field, (("wide", 0),), W)

    def fold_back(solved):
        owned = solved[W : W + block_x]
        for offset in (1, -1):
            rim_piece = solved[W + block_x :] if offset == 1 else solved[:W]
            arrived = passed_along(rim_piece, "wide", offset)
            if offset == 1:
                owned = owned + jnp.pad(arrived, ((0, block_x - W), (0, 0), (0, 0)))
            else:
                owned = owned + jnp.pad(arrived, ((block_x - W, 0), (0, 0), (0, 0)))
        return owned

    slot = lax.axis_index("wide") * lax.axis_size("narrow") + lax.axis_index("narrow")

    def placed_means(field):
        along_x = field.reshape(2, block_x // 2, block_y, block_z).sum(axis=1)
        along_y = along_x.reshape(2, 2, block_y // 2, block_z).sum(axis=2)
        along_z = along_y.reshape(2, 2, 2, block_z // 2).sum(axis=3)
        octant_means = (along_z / ((block_x // 2) * (block_y // 2) * (block_z // 2))).reshape(PRIMAL)
        return lax.dynamic_update_slice(
            jnp.zeros((coarse_rows.shape[1],), octant_means.dtype), octant_means, (slot * PRIMAL,)
        )

    def precondition(field, all_means, extended=None):
        if extended is None:
            extended = widen(transform_cross(field, table_y, table_z))
        coeffs = transform_first(extended, table_x) / spectrum
        local_part = transform_cross(fold_back(transform_first(coeffs, table_x)), table_y, table_z)
        correction = jnp.dot(coarse_rows, all_means, precision=lax.Precision.HIGHEST).reshape(
            2, 2, 2
        )
        upper_z = lax.broadcasted_iota(jnp.int32, (1, 1, block_z), 2) >= block_z // 2
        rows = jnp.where(upper_z, correction[:, :, 1:2], correction[:, :, 0:1])
        spread = jnp.broadcast_to(
            rows[:, None, :, None, :], (2, block_x // 2, 2, block_y // 2, block_z)
        )
        return local_part + spread.reshape(block_x, block_y, block_z)

    def apply_matrix(field):
        padded_field = with_cross_halo(field)
        return operate(field, padded_field, reaction, face_x, face_y, face_z)

    residual = source
    residual_means = total_over(placed_means(residual))
    preconditioned = precondition(residual, residual_means, first_extended)
    bent = apply_matrix(preconditioned)
    sums = total_over(
        jnp.concatenate(
            [
                jnp.stack([jnp.sum(residual * preconditioned), jnp.sum(preconditioned * bent)]),
                placed_means(bent),
            ]
        )
    )
    gamma_now, curvature, image_means = sums[0], sums[1], sums[2:]
    direction, image = preconditioned, bent
    step_size = gamma_now / curvature
    solution = step_size * direction
    residual = residual - step_size * image
    residual_means = residual_means - step_size * image_means
    for iteration in range(1, ITERS):
        preconditioned = precondition(residual, residual_means)
        bent = apply_matrix(preconditioned)
        sums = total_over(
            jnp.concatenate(
                [
                    jnp.stack(
                        [
                            jnp.sum(residual * preconditioned),
                            jnp.sum(preconditioned * bent),
                            jnp.sum(preconditioned * image),
                            jnp.sum(direction * bent),
                        ]
                    ),
                    placed_means(bent),
                ]
            )
        )
        gamma_next = sums[0]
        ratio = gamma_next / gamma_now
        curvature = sums[1] + ratio * (sums[2] + sums[3]) + ratio * ratio * curvature
        direction = preconditioned + ratio * direction
        image = bent + ratio * image
        image_means = sums[4:] + ratio * image_means
        gamma_now = gamma_next
        step_size = gamma_now / curvature
        solution = solution + step_size * direction
        residual = residual - step_size * image
        residual_means = residual_means - step_size * image_means
    preconditioned = precondition(residual, residual_means)
    gamma_next = total_over(jnp.sum(residual * preconditioned))
    direction = preconditioned + gamma_next / gamma_now * direction
    return (solution, residual, direction)


def solution(mesh):
    in_specs = (
        P("wide", "narrow", None),
        P("wide", "narrow", None),
        P("wide", "narrow", None),
        P("wide", "narrow", None, None),
    )
    out_specs = (P("wide", "narrow", None), P("wide", "narrow", None), P("wide", "narrow", None))
    return jax.shard_map(body, mesh=mesh, in_specs=in_specs, out_specs=out_specs, check_vma=False)
```
